512 devices in a mesh: wide: 32 (over y, x, core), grp: 16 (over z).
Axes of the slice: x: 4, y: 4, z: 16, core: 2. Of those that a mesh axis runs over, the one named last changes fastest.
Arguments:
- embeds: bfloat16 [147456, 1024], P(('wide', 'grp')), may hold values from -700 to 700
- bucket: int32 [147456], P(('wide', 'grp')), may hold values from 0 to 31, as said below
- pairs: int32 [8192], P(('wide', 'grp')), may hold values from -1 to 15, as said below
Outputs:
- density: float32 [512, 384], P(('wide', 'grp'))
The draws below stay inside these ranges and needn't reach their ends.
Inputs may be any that keep to these rules, and one draw needn't show every extreme that they name: At most 12 rows of one file shard name the same bucket; for every g some bucket is named by exactly 12 rows of every shard (s, g). `pairs`: the 16 entries of block (o, g) name distinct blocks (o, b) by b, live entries first and -1 after; for every o some block has all 16 entries live.
All inputs are finite; a program needn't handle non-finite values.
Results may differ from the reference program's by a relative error of at most 0.0034.
Values may be sent and summed in bfloat16 or wider, within the bound.
No kernel may reach another device: no remote copies, remote signals or barrier semaphores. Data moves between devices by JAX's collectives and lax.ppermute only.
A program may use at most 64 MiB of HBM per device.

```python
import jax
import jax.numpy as jnp
from jax import lax

D = 1024
BLK = 384
ROW_DEV = 288
CAP = 12
PAIR_DEV = 16
ROWS = 147456
N_WIDE = 32
N_GRP = 16


def distinct_order(rand_key, dimensions):
    length = dimensions[-1]
    raw_bits = jax.random.randint(rand_key, dimensions, 0, 1 << 20)
    scores = raw_bits * length + jnp.arange(length, dtype=jnp.int32)
    return jnp.argsort(scores, axis=-1).astype(jnp.int32)


def draw_embeds(key, part):
    topic_key, pick_key, jitter_key = jax.random.split(key, 3)
    topics = jnp.clip(jax.random.normal(topic_key, (64, D), jnp.float32), -4.0, 4.0)
    chosen = jax.random.randint(pick_key, (ROWS,), 0, 64)
    jitter = jnp.clip(jax.random.normal(jitter_key, (ROWS, D), jnp.float32), -4.0, 4.0)
    values = topics[chosen] + 0.6 * jitter
    return values.astype(jnp.bfloat16)


def draw_bucket(key, part):
    full_key, count_key, order_key, shuffle_key = jax.random.split(key, 4)
    shards = N_WIDE * N_GRP
    others = N_WIDE - 1
    remaining = ROW_DEV - CAP
    lowest = max(1, -(-remaining // others))
    full_bucket = jax.random.randint(full_key, (N_GRP,), 0, N_WIDE)
    full_shard = jnp.tile(full_bucket, N_WIDE)
    amounts = jax.random.randint(count_key, (shards, others), lowest, CAP + 1)
    running_total = jnp.cumsum(amounts, axis=1)
    positions = jnp.arange(remaining, dtype=jnp.int32)
    picked = jnp.sum((running_total[:, None, :] <= positions[None, :, None]).astype(jnp.int32), axis=2)
    ordering = distinct_order(order_key, (shards, others))
    chosen = jnp.take_along_axis(ordering, picked, axis=1)
    other_bucket = (full_shard[:, None] + 1 + chosen) % N_WIDE
    sequence = jnp.concatenate([jnp.broadcast_to(full_shard[:, None], (shards, CAP)), other_bucket], axis=1)
    shuffle = distinct_order(shuffle_key, (shards, ROW_DEV))
    return jnp.take_along_axis(sequence, shuffle, axis=1).reshape(-1).astype(jnp.int32)


def draw_pairs(key, part):
    order_key, live_key, full_key = jax.random.split(key, 3)
    shards = N_WIDE * N_GRP
    ordering = distinct_order(order_key, (shards, N_GRP))[:, :PAIR_DEV]
    divisor = 1 + jax.random.randint(live_key, (shards,), 0, 2)
    live_count = PAIR_DEV // divisor
    full_member = jax.random.randint(full_key, (N_WIDE,), 0, N_GRP)
    member_index = jnp.arange(shards, dtype=jnp.int32) % N_GRP
    busiest = jnp.repeat(full_member, N_GRP) == member_index
    live_count = jnp.where(busiest, PAIR_DEV, live_count)
    slot_index = jnp.arange(PAIR_DEV, dtype=jnp.int32)
    entries = jnp.where(slot_index[None, :] < live_count[:, None], ordering, -1)
    return entries.reshape(-1).astype(jnp.int32)


def setup_inputs(seed: int = 0) -> dict:
    seeds = jax.random.split(jax.random.key(seed), 4)
    return {
        "embeds": draw_embeds(jax.random.fold_in(seeds[3], 71), 0),
        "bucket": draw_bucket(jax.random.fold_in(seeds[3], 71), 0),
        "pairs": draw_pairs(jax.random.fold_in(seeds[3], 71), 0),
    }


SHARPNESS = 10.0
EPSILON = 1e-06

def normalize(embeds):
    floats = embeds.astype(jnp.float32)
    return (floats * lax.rsqrt(lax.optimization_barrier(jnp.sum(floats * floats, axis=1, keepdims=True)) + EPSILON)).astype(jnp.bfloat16)

def reference(embeds, bucket, pairs):
    unit_rows = normalize(embeds).reshape(N_WIDE, N_GRP, ROW_DEV, D)
    owners = bucket.reshape(N_WIDE, N_GRP, ROW_DEV)
    onehot = (owners[..., None] == jnp.arange(N_WIDE, dtype=jnp.int32)).astype(jnp.int32)
    row_ranks = lax.optimization_barrier(jnp.sum(jnp.cumsum(onehot, axis=2) * onehot, axis=3)) - 1
    counts = lax.optimization_barrier(jnp.sum(onehot, axis=2))
    offsets = jnp.cumsum(counts, axis=0) - counts
    starts = jnp.take_along_axis(offsets, owners, axis=2)
    positions = (starts + row_ranks).astype(jnp.int32)
    totals = lax.optimization_barrier(jnp.sum(counts, axis=0)).T
    member = jnp.broadcast_to(jnp.arange(N_GRP, dtype=jnp.int32)[None, :, None], owners.shape)
    blocks = jnp.zeros((N_WIDE, N_GRP, BLK, D), jnp.bfloat16).at[owners, member, positions].set(unit_rows)
    valid_rows = (jnp.arange(BLK, dtype=jnp.int32)[None, None, :] < totals[:, :, None]).astype(jnp.float32)
    pair_lists = pairs.reshape(N_WIDE, N_GRP, PAIR_DEV)

    def one_owner(operands):
        owner_blocks, owner_flags, owner_lists = operands

        def one_shard(pieces):
            own_block, row_flags, entries = pieces
            live_count = jnp.sum((entries >= 0).astype(jnp.int32))
            left_rows = own_block.astype(jnp.float32)

            def add_pair(pair_index, running):
                target = entries[pair_index].astype(jnp.int32)
                right_rows = lax.dynamic_index_in_dim(owner_blocks, target, 0, keepdims=False).astype(jnp.float32)
                right_flags = lax.dynamic_index_in_dim(owner_flags, target, 0, keepdims=False)
                cosines = jnp.dot(left_rows, right_rows.T, precision=lax.Precision.HIGHEST)
                return running + lax.optimization_barrier(jnp.sum(jnp.exp(SHARPNESS * (cosines - 1.0)) * right_flags[None, :], axis=1))
            summed = lax.fori_loop(0, live_count, add_pair, jnp.zeros((BLK,), jnp.float32))
            return summed * row_flags
        return lax.map(one_shard, (owner_blocks, owner_flags, owner_lists))
    density = lax.map(one_owner, (blocks, valid_rows, pair_lists))
    return density.reshape(N_WIDE * N_GRP, BLK)
```

```python
import jax
import jax.numpy as jnp
from jax import lax
from jax.sharding import PartitionSpec as P

BLK = 384


SHARPNESS = 10.0
EPSILON = 1e-06
SENTINEL = 2.0


def pair_products(left_rows, right_rows):
    cosines = lax.dot_general(
        left_rows, right_rows, (((1,), (1,)), ((), ())), preferred_element_type=jnp.float32
    )
    return jnp.exp(SHARPNESS * (cosines - 1.0))


def per_device(embeds, bucket, pairs):
    wide_count = lax.axis_size("wide")
    grp_count = lax.axis_size("grp")
    feature_width = embeds.shape[1]
    capacity = BLK // wide_count
    me = lax.axis_index("grp")

    all_pairs = lax.all_gather(pairs, "grp", axis=0, tiled=False)
    blocks_iota = jnp.arange(grp_count, dtype=jnp.int32)
    member = jnp.any(all_pairs[:, :, None] == blocks_iota[None, None, :], axis=1).astype(jnp.float32)

    floats = embeds.astype(jnp.float32)
    unit_rows = (
        floats * lax.rsqrt(jnp.sum(floats * floats, axis=1, keepdims=True) + EPSILON)
    ).astype(jnp.bfloat16)
    onehot = (bucket[:, None] == jnp.arange(wide_count, dtype=jnp.int32)[None, :]).astype(jnp.int32)
    row_ranks = jnp.sum(jnp.cumsum(onehot, axis=0) * onehot, axis=1) - 1
    send_slots = bucket * capacity + row_ranks
    empty = jnp.zeros((wide_count * capacity, feature_width), jnp.bfloat16).at[:, 0].set(SENTINEL)
    outgoing = empty.at[send_slots].set(unit_rows)
    own = lax.all_to_all(
        outgoing.reshape(wide_count, capacity, feature_width),
        "wide",
        split_axis=0,
        concat_axis=0,
        tiled=True,
    ).reshape(BLK, feature_width)

    def valid_of(rows):
        return (rows[:, 0].astype(jnp.float32) < 1.5).astype(jnp.float32)

    from_left = [(i, (i + 1) % grp_count) for i in range(grp_count)]
    from_right = [(i, (i - 1) % grp_count) for i in range(grp_count)]
    left = {0: own}
    right = {0: own}
    for step in range(1, 5):
        left[step] = lax.ppermute(left[step - 1], "grp", from_left)
        right[step] = lax.ppermute(right[step - 1], "grp", from_right)
    rows_at = {0: own}
    for step in range(1, 5):
        rows_at[-step] = left[step]
        rows_at[step] = right[step]
    valid_at = {k: valid_of(v) for k, v in rows_at.items()}

    def block_at(k):
        return (me + k) % grp_count

    targets = []
    vectors = []
    e = pair_products(own, own)
    targets.append(block_at(0))
    vectors.append(jnp.sum(e * valid_at[0][None, :], axis=1) * member[me, me])
    half = grp_count // 2
    plan = [(0, 1), (0, 2), (0, 3), (0, 4), (-2, 3), (-3, 3), (-3, 4), (-4, 4)]
    for p, q in plan:
        a = block_at(p)
        b = block_at(q)
        e = pair_products(rows_at[p], rows_at[q])
        scale = jnp.float32(1.0)
        if q - p == half:
            scale = (me < half).astype(jnp.float32)
        to_a = jnp.sum(e * valid_at[q][None, :], axis=1) * (member[a, b] * scale)
        to_b = jnp.sum(e * valid_at[p][:, None], axis=0) * (member[b, a] * scale)
        targets += [a, b]
        vectors += [to_a, to_b]
    contrib = (
        jnp.zeros((grp_count, BLK), jnp.float32)
        .at[jnp.stack(targets)]
        .add(jnp.stack(vectors))
    )
    slot_sums = lax.psum_scatter(contrib, "grp", scatter_dimension=0, tiled=True).reshape(BLK)

    own_valid = valid_at[0].reshape(wide_count, capacity)
    arrived = jnp.sum(own_valid, axis=1).astype(jnp.int32)
    offsets = jnp.cumsum(arrived) - arrived
    within = jnp.arange(capacity, dtype=jnp.int32)
    places = jnp.where(own_valid > 0, offsets[:, None] + within[None, :], BLK).reshape(-1)
    density = jnp.zeros((BLK,), jnp.float32).at[places].set(slot_sums, mode="drop")
    return density.reshape(1, BLK)


def solution(mesh):
    placed = (P(("wide", "grp"), None), P(("wide", "grp")), P(("wide", "grp")))
    return jax.shard_map(
        per_device, mesh=mesh, in_specs=placed, out_specs=P(("wide", "grp"), None), check_vma=False
    )
```

```python
import jax
import jax.numpy as jnp
from jax import lax
from jax.sharding import PartitionSpec as P

BLK = 384


SHARPNESS = 10.0
EPSILON = 1e-06
SENTINEL = 2.0


def pair_products(left_rows, right_rows):
    cosines = lax.dot_general(
        left_rows, right_rows, (((1,), (1,)), ((), ())), preferred_element_type=jnp.float32
    )
    return jnp.exp(SHARPNESS * (cosines - 1.0))


def per_device(embeds, bucket, pairs):
    wide_count = lax.axis_size("wide")
    grp_count = lax.axis_size("grp")
    feature_width = embeds.shape[1]
    capacity = BLK // wide_count
    me = lax.axis_index("grp")

    blocks_iota = jnp.arange(grp_count, dtype=jnp.int32)
    member = jnp.any(pairs[:, None] == blocks_iota[None, :], axis=0).astype(jnp.float32)

    floats = embeds.astype(jnp.float32)
    unit_rows = (
        floats * lax.rsqrt(jnp.sum(floats * floats, axis=1, keepdims=True) + EPSILON)
    ).astype(jnp.bfloat16)
    onehot = (bucket[:, None] == jnp.arange(wide_count, dtype=jnp.int32)[None, :]).astype(jnp.int32)
    row_ranks = jnp.sum(jnp.cumsum(onehot, axis=0) * onehot, axis=1) - 1
    send_slots = bucket * capacity + row_ranks
    empty = jnp.zeros((wide_count * capacity, feature_width), jnp.bfloat16).at[:, 0].set(SENTINEL)
    outgoing = empty.at[send_slots].set(unit_rows)
    own = lax.all_to_all(
        outgoing.reshape(wide_count, capacity, feature_width),
        "wide",
        split_axis=0,
        concat_axis=0,
        tiled=True,
    ).reshape(BLK, feature_width)

    def valid_of(rows):
        return (rows[:, 0].astype(jnp.float32) < 1.5).astype(jnp.float32)

    def shift(value, offset):
        return lax.ppermute(
            value, "grp", [(i, (i + offset) % grp_count) for i in range(grp_count)]
        )

    reach = 4
    left = {0: own}
    right = {0: own}
    for step in range(1, reach + 1):
        left[step] = shift(left[step - 1], 1)
        right[step] = shift(right[step - 1], -1)
    rows_at = {0: own}
    for step in range(1, reach + 1):
        rows_at[-step] = left[step]
        rows_at[step] = right[step]
    valid_at = {k: valid_of(v) for k, v in rows_at.items()}

    outgoing_sums = {}

    def add(target, source, sums):
        outgoing_sums.setdefault(target, []).append((source, sums))

    e = pair_products(own, own)
    add(0, 0, jnp.sum(e * valid_at[0][None, :], axis=1))
    half = grp_count // 2
    plan = [(0, 1), (0, 2), (0, 3), (0, 4), (-2, 3), (-3, 3), (-3, 4), (-4, 4)]
    for p, q in plan:
        e = pair_products(rows_at[p], rows_at[q])
        to_p = jnp.sum(e * valid_at[q][None, :], axis=1)
        to_q = jnp.sum(e * valid_at[p][:, None], axis=0)
        if q - p == half:
            keep = (me < half).astype(jnp.float32)
            to_p = to_p * keep
            to_q = to_q * keep
        add(p, q, to_p)
        add(q, p, to_q)

    slot_sums = jnp.zeros((BLK,), jnp.float32)
    for target, items in sorted(outgoing_sums.items()):
        stacked = jnp.stack([sums for _, sums in items])
        if target != 0:
            stacked = shift(stacked, target)
        sources = (me + jnp.array([s - target for s, _ in items], jnp.int32)) % grp_count
        slot_sums = slot_sums + jnp.sum(stacked * member[sources][:, None], axis=0)

    own_valid = valid_at[0].reshape(wide_count, capacity)
    arrived = jnp.sum(own_valid, axis=1).astype(jnp.int32)
    offsets = jnp.cumsum(arrived) - arrived
    within = jnp.arange(capacity, dtype=jnp.int32)
    places = jnp.where(own_valid > 0, offsets[:, None] + within[None, :], BLK).reshape(-1)
    density = jnp.zeros((BLK,), jnp.float32).at[places].set(slot_sums, mode="drop")
    return density.reshape(1, BLK)


def solution(mesh):
    placed = (P(("wide", "grp"), None), P(("wide", "grp")), P(("wide", "grp")))
    return jax.shard_map(
        per_device, mesh=mesh, in_specs=placed, out_specs=P(("wide", "grp"), None), check_vma=False
    )
```

```python
import jax
import jax.numpy as jnp
from jax import lax
from jax.sharding import PartitionSpec as P

BLK = 384


SHARPNESS = 10.0
EPSILON = 1e-06
SENTINEL = 2.0


def pair_products(left_rows, right_rows):
    cosines = lax.dot_general(
        left_rows, right_rows, (((1,), (1,)), ((), ())), preferred_element_type=jnp.float32
    )
    return jnp.exp(SHARPNESS * (cosines - 1.0))


def per_device(embeds, bucket, pairs):
    wide_count = lax.axis_size("wide")
    grp_count = lax.axis_size("grp")
    feature_width = embeds.shape[1]
    capacity = BLK // wide_count
    me = lax.axis_index("grp")

    blocks_iota = jnp.arange(grp_count, dtype=jnp.int32)
    member = jnp.any(pairs[:, None] == blocks_iota[None, :], axis=0).astype(jnp.float32)

    floats = embeds.astype(jnp.float32)
    unit_rows = (
        floats * lax.rsqrt(jnp.sum(floats * floats, axis=1, keepdims=True) + EPSILON)
    ).astype(jnp.bfloat16)
    onehot = (bucket[:, None] == jnp.arange(wide_count, dtype=jnp.int32)[None, :]).astype(jnp.int32)
    row_ranks = jnp.sum(jnp.cumsum(onehot, axis=0) * onehot, axis=1) - 1
    send_slots = bucket * capacity + row_ranks
    empty = jnp.zeros((wide_count * capacity, feature_width), jnp.bfloat16).at[:, 0].set(SENTINEL)
    outgoing = empty.at[send_slots].set(unit_rows)
    own = lax.all_to_all(
        outgoing.reshape(wide_count, capacity, feature_width),
        "wide",
        split_axis=0,
        concat_axis=0,
        tiled=True,
    ).reshape(BLK, feature_width)

    def valid_of(rows):
        return (rows[:, 0].astype(jnp.float32) < 1.5).astype(jnp.float32)

    def shift(value, offset):
        return lax.ppermute(
            value, "grp", [(i, (i + offset) % grp_count) for i in range(grp_count)]
        )

    reach = 4
    left = {0: own}
    right = {0: own}
    for step in range(1, reach + 1):
        left[step] = shift(left[step - 1], 1)
        right[step] = shift(right[step - 1], -1)
    rows_at = {0: own}
    for step in range(1, reach + 1):
        rows_at[-step] = left[step]
        rows_at[step] = right[step]
    valid_at = {k: valid_of(v) for k, v in rows_at.items()}

    outgoing_sums = {}

    def add(target, source, sums):
        outgoing_sums.setdefault(target, []).append((source, sums))

    e = pair_products(own, own)
    add(0, 0, jnp.sum(e * valid_at[0][None, :], axis=1))
    half = grp_count // 2
    plan = [(0, 1), (0, 2), (0, 3), (0, 4), (-2, 3), (-3, 3), (-3, 4), (-4, 4)]
    for p, q in plan:
        e = pair_products(rows_at[p], rows_at[q])
        to_p = jnp.sum(e * valid_at[q][None, :], axis=1)
        to_q = jnp.sum(e * valid_at[p][:, None], axis=0)
        if q - p == half:
            keep = (me < half).astype(jnp.float32)
            to_p = to_p * keep
            to_q = to_q * keep
        add(p, q, to_p)
        add(q, p, to_q)

    depth = max(len(items) for t, items in outgoing_sums.items() if t != 0)
    zero = jnp.zeros((BLK,), jnp.float32)
    table = [[zero] * depth for _ in range(grp_count)]
    source_table = [[0] * depth for _ in range(grp_count)]
    present_table = [[0.0] * depth for _ in range(grp_count)]
    for target, items in outgoing_sums.items():
        if target == 0:
            continue
        for k, (source, sums) in enumerate(items):
            table[target % grp_count][k] = sums
            source_table[target % grp_count][k] = source - target
            present_table[target % grp_count][k] = 1.0
    by_offset = jnp.stack([jnp.stack(row) for row in table])
    by_device = by_offset[(blocks_iota - me) % grp_count]
    arrived_sums = lax.all_to_all(by_device, "grp", split_axis=0, concat_axis=0, tiled=True)
    offset_of_sender = (me - blocks_iota) % grp_count
    sources = (me + jnp.array(source_table, jnp.int32)[offset_of_sender]) % grp_count
    weights = member[sources] * jnp.array(present_table, jnp.float32)[offset_of_sender]
    slot_sums = jnp.sum(arrived_sums * weights[:, :, None], axis=(0, 1))
    for source, sums in outgoing_sums[0]:
        slot_sums = slot_sums + sums * member[(me + source) % grp_count]

    own_valid = valid_at[0].reshape(wide_count, capacity)
    arrived = jnp.sum(own_valid, axis=1).astype(jnp.int32)
    offsets = jnp.cumsum(arrived) - arrived
    within = jnp.arange(capacity, dtype=jnp.int32)
    places = jnp.where(own_valid > 0, offsets[:, None] + within[None, :], BLK).reshape(-1)
    density = jnp.zeros((BLK,), jnp.float32).at[places].set(slot_sums, mode="drop")
    return density.reshape(1, BLK)


def solution(mesh):
    placed = (P(("wide", "grp"), None), P(("wide", "grp")), P(("wide", "grp")))
    return jax.shard_map(
        per_device, mesh=mesh, in_specs=placed, out_specs=P(("wide", "grp"), None), check_vma=False
    )
```

```python
import jax
import jax.numpy as jnp
from jax import lax
from jax.sharding import PartitionSpec as P

BLK = 384


SHARPNESS = 10.0
EPSILON = 1e-06
SENTINEL = 2.0


def pair_products(left_rows, right_rows):
    cosines = lax.dot_general(
        left_rows, right_rows, (((1,), (1,)), ((), ())), preferred_element_type=jnp.float32
    )
    return jnp.exp(SHARPNESS * (cosines - 1.0))


def per_device(embeds, bucket, pairs):
    wide_count = lax.axis_size("wide")
    grp_count = lax.axis_size("grp")
    feature_width = embeds.shape[1]
    capacity = BLK // wide_count
    me = lax.axis_index("grp")

    blocks_iota = jnp.arange(grp_count, dtype=jnp.int32)
    member = jnp.any(pairs[:, None] == blocks_iota[None, :], axis=0).astype(jnp.float32)

    floats = embeds.astype(jnp.float32)
    unit_rows = (
        floats * lax.rsqrt(jnp.sum(floats * floats, axis=1, keepdims=True) + EPSILON)
    ).astype(jnp.bfloat16)
    onehot = (bucket[:, None] == jnp.arange(wide_count, dtype=jnp.int32)[None, :]).astype(jnp.int32)
    row_ranks = jnp.sum(jnp.cumsum(onehot, axis=0) * onehot, axis=1) - 1
    send_slots = bucket * capacity + row_ranks
    empty = jnp.zeros((wide_count * capacity, feature_width), jnp.bfloat16).at[:, 0].set(SENTINEL)
    outgoing = empty.at[send_slots].set(unit_rows).reshape(wide_count, capacity, feature_width)
    split = capacity // 2
    halves = [outgoing[:, :split], outgoing[:, split:]]
    own_halves = [
        lax.all_to_all(h, "wide", split_axis=0, concat_axis=0, tiled=True).reshape(-1, feature_width)
        for h in halves
    ]

    def valid_of(rows):
        return (rows[:, 0].astype(jnp.float32) < 1.5).astype(jnp.float32)

    def shift(value, offset):
        return lax.ppermute(
            value, "grp", [(i, (i + offset) % grp_count) for i in range(grp_count)]
        )

    reach = 4
    rows_at = {}
    for part in own_halves:
        left = part
        right = part
        rows_at.setdefault(0, []).append(part)
        for step in range(1, reach + 1):
            left = shift(left, 1)
            right = shift(right, -1)
            rows_at.setdefault(-step, []).append(left)
            rows_at.setdefault(step, []).append(right)
    rows_at = {k: jnp.concatenate(v, axis=0) for k, v in rows_at.items()}
    own = rows_at[0]
    valid_at = {k: valid_of(v) for k, v in rows_at.items()}

    outgoing_sums = {}

    def add(target, source, sums):
        outgoing_sums.setdefault(target, []).append((source, sums))

    e = pair_products(own, own)
    add(0, 0, jnp.sum(e * valid_at[0][None, :], axis=1))
    half = grp_count // 2
    plan = [(0, 1), (0, 2), (0, 3), (0, 4), (-2, 3), (-3, 3), (-3, 4), (-4, 4)]
    for p, q in plan:
        e = pair_products(rows_at[p], rows_at[q])
        to_p = jnp.sum(e * valid_at[q][None, :], axis=1)
        to_q = jnp.sum(e * valid_at[p][:, None], axis=0)
        if q - p == half:
            keep = (me < half).astype(jnp.float32)
            to_p = to_p * keep
            to_q = to_q * keep
        add(p, q, to_p)
        add(q, p, to_q)

    depth = max(len(items) for t, items in outgoing_sums.items() if t != 0)
    zero = jnp.zeros((BLK,), jnp.float32)
    table = [[zero] * depth for _ in range(grp_count)]
    source_table = [[0] * depth for _ in range(grp_count)]
    present_table = [[0.0] * depth for _ in range(grp_count)]
    for target, items in outgoing_sums.items():
        if target == 0:
            continue
        for k, (source, sums) in enumerate(items):
            table[target % grp_count][k] = sums
            source_table[target % grp_count][k] = source - target
            present_table[target % grp_count][k] = 1.0
    by_offset = jnp.stack([jnp.stack(row) for row in table])
    by_device = by_offset[(blocks_iota - me) % grp_count]
    arrived_sums = lax.all_to_all(by_device, "grp", split_axis=0, concat_axis=0, tiled=True)
    offset_of_sender = (me - blocks_iota) % grp_count
    sources = (me + jnp.array(source_table, jnp.int32)[offset_of_sender]) % grp_count
    weights = member[sources] * jnp.array(present_table, jnp.float32)[offset_of_sender]
    slot_sums = jnp.sum(arrived_sums * weights[:, :, None], axis=(0, 1))
    for source, sums in outgoing_sums[0]:
        slot_sums = slot_sums + sums * member[(me + source) % grp_count]

    own_valid = valid_at[0].reshape(2, wide_count, split).transpose(1, 0, 2).reshape(wide_count, capacity)
    arrived = jnp.sum(own_valid, axis=1).astype(jnp.int32)
    offsets = jnp.cumsum(arrived) - arrived
    within = jnp.arange(capacity, dtype=jnp.int32)
    places = jnp.where(own_valid > 0, offsets[:, None] + within[None, :], BLK)
    places = places.reshape(wide_count, 2, split).transpose(1, 0, 2).reshape(-1)
    density = jnp.zeros((BLK,), jnp.float32).at[places].set(slot_sums, mode="drop")
    return density.reshape(1, BLK)


def solution(mesh):
    placed = (P(("wide", "grp"), None), P(("wide", "grp")), P(("wide", "grp")))
    return jax.shard_map(
        per_device, mesh=mesh, in_specs=placed, out_specs=P(("wide", "grp"), None), check_vma=False
    )
```

```python
import jax
import jax.numpy as jnp
from jax import lax
from jax.sharding import PartitionSpec as P

BLK = 384


SHARPNESS = 10.0
EPSILON = 1e-06
SENTINEL = 2.0


def pair_products(left_rows, right_rows):
    cosines = lax.dot_general(
        left_rows, right_rows, (((1,), (1,)), ((), ())), preferred_element_type=jnp.float32
    )
    return jnp.exp(SHARPNESS * (cosines - 1.0))


def per_device(embeds, bucket, pairs):
    wide_count = lax.axis_size("wide")
    grp_count = lax.axis_size("grp")
    feature_width = embeds.shape[1]
    capacity = BLK // wide_count
    me = lax.axis_index("grp")

    blocks_iota = jnp.arange(grp_count, dtype=jnp.int32)
    member = jnp.any(pairs[:, None] == blocks_iota[None, :], axis=0).astype(jnp.float32)

    floats = embeds.astype(jnp.float32)
    unit_rows = (
        floats * lax.rsqrt(jnp.sum(floats * floats, axis=1, keepdims=True) + EPSILON)
    ).astype(jnp.bfloat16)
    onehot = (bucket[:, None] == jnp.arange(wide_count, dtype=jnp.int32)[None, :]).astype(jnp.int32)
    row_ranks = jnp.sum(jnp.cumsum(onehot, axis=0) * onehot, axis=1) - 1
    send_slots = bucket * capacity + row_ranks
    empty = jnp.zeros((wide_count * capacity, feature_width), jnp.bfloat16).at[:, 0].set(SENTINEL)
    outgoing = empty.at[send_slots].set(unit_rows).reshape(wide_count, capacity, feature_width)
    split = capacity // 2
    halves = [outgoing[:, :split], outgoing[:, split:]]
    own_halves = [
        lax.all_to_all(h, "wide", split_axis=0, concat_axis=0, tiled=True).reshape(-1, feature_width)
        for h in halves
    ]

    def valid_of(rows):
        return (rows[:, 0].astype(jnp.float32) < 1.5).astype(jnp.float32)

    def shift(value, offset):
        return lax.ppermute(
            value, "grp", [(i, (i + offset) % grp_count) for i in range(grp_count)]
        )

    reach = 4
    rows_at = {}
    for part in own_halves:
        left = part
        right = part
        rows_at.setdefault(0, []).append(part)
        for step in range(1, reach + 1):
            left = shift(left, 1)
            right = shift(right, -1)
            rows_at.setdefault(-step, []).append(left)
            rows_at.setdefault(step, []).append(right)
    rows_at = {k: jnp.concatenate(v, axis=0) for k, v in rows_at.items()}
    own = rows_at[0]
    valid_at = {k: valid_of(v) for k, v in rows_at.items()}

    outgoing_sums = {}

    def add(target, source, sums):
        outgoing_sums.setdefault(target, []).append((source, sums))

    e = pair_products(own, own)
    add(0, 0, jnp.sum(e * valid_at[0][None, :], axis=1))
    half = grp_count // 2
    plan = [(0, 1), (0, 2), (0, 3), (0, 4), (-2, 3), (-3, 3), (-3, 4), (-4, 4)]
    for p, q in plan:
        e = pair_products(rows_at[p], rows_at[q])
        to_p = jnp.sum(e * valid_at[q][None, :], axis=1)
        to_q = jnp.sum(e * valid_at[p][:, None], axis=0)
        if q - p == half:
            keep = (me < half).astype(jnp.float32)
            to_p = to_p * keep
            to_q = to_q * keep
        add(p, q, to_p)
        add(q, p, to_q)

    packed = []
    target_table = []
    source_table = []
    for target, items in sorted(outgoing_sums.items()):
        if target == 0:
            continue
        for source, sums in items:
            packed.append(sums)
            target_table.append(target % grp_count)
            source_table.append(source - target)
    gathered = lax.all_gather(jnp.stack(packed), "grp", axis=0, tiled=False)
    offset_of_sender = (me - blocks_iota) % grp_count
    meant = offset_of_sender[:, None] == jnp.array(target_table, jnp.int32)[None, :]
    sources = (me + jnp.array(source_table, jnp.int32)) % grp_count
    weights = jnp.where(meant, member[sources][None, :], 0.0)
    slot_sums = jnp.sum(gathered * weights[:, :, None], axis=(0, 1))
    for source, sums in outgoing_sums[0]:
        slot_sums = slot_sums + sums * member[(me + source) % grp_count]

    own_valid = valid_at[0].reshape(2, wide_count, split).transpose(1, 0, 2).reshape(wide_count, capacity)
    arrived = jnp.sum(own_valid, axis=1).astype(jnp.int32)
    offsets = jnp.cumsum(arrived) - arrived
    within = jnp.arange(capacity, dtype=jnp.int32)
    places = jnp.where(own_valid > 0, offsets[:, None] + within[None, :], BLK)
    places = places.reshape(wide_count, 2, split).transpose(1, 0, 2).reshape(-1)
    rows_iota = jnp.arange(BLK, dtype=jnp.int32)
    density = jnp.sum(jnp.where(places[:, None] == rows_iota[None, :], slot_sums[:, None], 0.0), axis=0)
    return density.reshape(1, BLK)


def solution(mesh):
    placed = (P(("wide", "grp"), None), P(("wide", "grp")), P(("wide", "grp")))
    return jax.shard_map(
        per_device, mesh=mesh, in_specs=placed, out_specs=P(("wide", "grp"), None), check_vma=False
    )
```

```python
import jax
import jax.numpy as jnp
from jax import lax
from jax.sharding import PartitionSpec as P


BLK = 384


SHARPNESS = 10.0
EPSILON = 1e-06
SENTINEL = 2.0


def pair_products(left_rows, right_rows):
    cosines = lax.dot_general(
        left_rows, right_rows, (((1,), (1,)), ((), ())), preferred_element_type=jnp.float32
    )
    return jnp.exp(SHARPNESS * (cosines - 1.0))


def per_device(embeds, bucket, pairs):
    wide_count = lax.axis_size("wide")
    grp_count = lax.axis_size("grp")
    feature_width = embeds.shape[1]
    capacity = BLK // wide_count
    me = lax.axis_index("grp")

    blocks_iota = jnp.arange(grp_count, dtype=jnp.int32)
    member = jnp.any(pairs[:, None] == blocks_iota[None, :], axis=0).astype(jnp.float32)

    floats = embeds.astype(jnp.float32)
    unit_rows = (
        floats * lax.rsqrt(jnp.sum(floats * floats, axis=1, keepdims=True) + EPSILON)
    ).astype(jnp.bfloat16)
    onehot = (bucket[:, None] == jnp.arange(wide_count, dtype=jnp.int32)[None, :]).astype(jnp.int32)
    row_ranks = jnp.sum(jnp.cumsum(onehot, axis=0) * onehot, axis=1) - 1
    send_slots = bucket * capacity + row_ranks
    empty = jnp.zeros((wide_count * capacity, feature_width), jnp.bfloat16).at[:, 0].set(SENTINEL)
    outgoing = empty.at[send_slots].set(unit_rows).reshape(wide_count, capacity, feature_width)
    split = capacity // 2
    halves = [outgoing[:, :split], outgoing[:, split:]]
    own_halves = [
        lax.all_to_all(h, "wide", split_axis=0, concat_axis=0, tiled=True).reshape(-1, feature_width)
        for h in halves
    ]

    def valid_of(rows):
        return (rows[:, 0].astype(jnp.float32) < 1.5).astype(jnp.float32)

    def shift(value, offset):
        return lax.ppermute(
            value, "grp", [(i, (i + offset) % grp_count) for i in range(grp_count)]
        )

    reach = 4
    rows_at = {}
    for part in own_halves:
        left = part
        right = part
        rows_at.setdefault(0, []).append(part)
        for step in range(1, reach + 1):
            left = shift(left, 1)
            right = shift(right, -1)
            rows_at.setdefault(-step, []).append(left)
            rows_at.setdefault(step, []).append(right)
    halves_at = rows_at
    rows_at = {}
    valid_at = {}
    for k, v in halves_at.items():
        rows_at[k] = jnp.concatenate(v, axis=0)
        valid_at[k] = valid_of(rows_at[k])
    own = rows_at[0]

    early = {}
    late = {}

    def add(sums_by_target, target, source, sums):
        sums_by_target.setdefault(target, []).append((source, sums))

    e = pair_products(own, own)
    add(early, 0, 0, jnp.sum(e * valid_at[0][None, :], axis=1))
    plan = [(0, 1), (0, 2), (0, 3), (-2, 2), (-2, 3), (-3, 3), (-4, 3)]
    for p, q in plan:
        e = pair_products(rows_at[p], rows_at[q])
        to_p = jnp.sum(e * valid_at[q][None, :], axis=1)
        to_q = jnp.sum(e * valid_at[p][:, None], axis=0)
        group = late if max(-p, q) == reach else early
        add(group, p, q, to_p)
        add(group, q, p, to_q)
    e = pair_products(rows_at[-reach], rows_at[reach])
    add(late, -reach, reach, jnp.sum(e * valid_at[reach][None, :], axis=1))

    def weighted(stacked, items, target):
        sources = (me + jnp.array([s - target for s, _ in items], jnp.int32)) % grp_count
        return jnp.sum(stacked * member[sources][:, None], axis=0)

    slot_sums = weighted(jnp.stack([s for _, s in early[0]]), early[0], 0)

    depth = max(len(items) for t, items in early.items() if t != 0)
    zero = jnp.zeros((BLK,), jnp.float32)
    table = [[zero] * depth for _ in range(grp_count)]
    source_table = [[0] * depth for _ in range(grp_count)]
    present_table = [[0.0] * depth for _ in range(grp_count)]
    for target, items in early.items():
        if target == 0:
            continue
        for k, (source, sums) in enumerate(items):
            table[target % grp_count][k] = sums
            source_table[target % grp_count][k] = source - target
            present_table[target % grp_count][k] = 1.0
    by_offset = jnp.stack([jnp.stack(row) for row in table])
    by_device = by_offset[(blocks_iota - me) % grp_count]
    arrived_sums = lax.all_to_all(by_device, "grp", split_axis=0, concat_axis=0, tiled=True)
    offset_of_sender = (me - blocks_iota) % grp_count
    sources = (me + jnp.array(source_table, jnp.int32)[offset_of_sender]) % grp_count
    weights = member[sources] * jnp.array(present_table, jnp.float32)[offset_of_sender]
    slot_sums = slot_sums + jnp.sum(arrived_sums * weights[:, :, None], axis=(0, 1))

    for target, items in sorted(late.items()):
        stacked = shift(jnp.stack([s for _, s in items]), target)
        slot_sums = slot_sums + weighted(stacked, items, target)

    own_valid = valid_at[0].reshape(2, wide_count, split).transpose(1, 0, 2).reshape(wide_count, capacity)
    arrived = jnp.sum(own_valid, axis=1).astype(jnp.int32)
    offsets = jnp.cumsum(arrived) - arrived
    within = jnp.arange(capacity, dtype=jnp.int32)
    places = jnp.where(own_valid > 0, offsets[:, None] + within[None, :], BLK)
    places = places.reshape(wide_count, 2, split).transpose(1, 0, 2).reshape(-1)
    rows_iota = jnp.arange(BLK, dtype=jnp.int32)
    density = jnp.sum(jnp.where(places[:, None] == rows_iota[None, :], slot_sums[:, None], 0.0), axis=0)
    return density.reshape(1, BLK)


def solution(mesh):
    placed = (P(("wide", "grp"), None), P(("wide", "grp")), P(("wide", "grp")))
    return jax.shard_map(per_device, mesh=mesh, in_specs=placed, out_specs=P(("wide", "grp"), None), check_vma=False)
```

```python
import jax
import jax.numpy as jnp
from jax import lax
from jax.sharding import PartitionSpec as P


BLK = 384


SHARPNESS = 10.0
EPSILON = 1e-06
SENTINEL = 2.0


def pair_products(left_rows, right_rows):
    cosines = lax.dot_general(
        left_rows, right_rows, (((1,), (1,)), ((), ())), preferred_element_type=jnp.float32
    )
    return jnp.exp(SHARPNESS * (cosines - 1.0))


def per_device(embeds, bucket, pairs):
    wide_count = lax.axis_size("wide")
    grp_count = lax.axis_size("grp")
    feature_width = embeds.shape[1]
    capacity = BLK // wide_count
    me = lax.axis_index("grp")

    blocks_iota = jnp.arange(grp_count, dtype=jnp.int32)
    member = jnp.any(pairs[:, None] == blocks_iota[None, :], axis=0).astype(jnp.float32)

    floats = embeds.astype(jnp.float32)
    unit_rows = (
        floats * lax.rsqrt(jnp.sum(floats * floats, axis=1, keepdims=True) + EPSILON)
    ).astype(jnp.bfloat16)
    onehot = (bucket[:, None] == jnp.arange(wide_count, dtype=jnp.int32)[None, :]).astype(jnp.int32)
    row_ranks = jnp.sum(jnp.cumsum(onehot, axis=0) * onehot, axis=1) - 1
    send_slots = bucket * capacity + row_ranks
    empty = jnp.zeros((wide_count * capacity, feature_width), jnp.bfloat16).at[:, 0].set(SENTINEL)
    outgoing = empty.at[send_slots].set(unit_rows).reshape(wide_count, capacity, feature_width)
    split = capacity // 2
    halves = [outgoing[:, :split], outgoing[:, split:]]
    lanes = 128
    own_halves = [
        lax.all_to_all(
            h.reshape(wide_count, -1, lanes), "wide", split_axis=0, concat_axis=0, tiled=True
        ).reshape(-1, feature_width)
        for h in halves
    ]

    def valid_of(rows):
        return (rows[:, 0].astype(jnp.float32) < 1.5).astype(jnp.float32)

    def shift(value, offset):
        return lax.ppermute(
            value, "grp", [(i, (i + offset) % grp_count) for i in range(grp_count)]
        )

    reach = 4
    rows_at = {}
    for part in own_halves:
        left = part
        right = part
        rows_at.setdefault(0, []).append(part)
        for step in range(1, reach + 1):
            left = shift(left, 1)
            right = shift(right, -1)
            rows_at.setdefault(-step, []).append(left)
            rows_at.setdefault(step, []).append(right)
    halves_at = rows_at
    rows_at = {}
    valid_at = {}
    for k, v in halves_at.items():
        rows_at[k] = jnp.concatenate(v, axis=0)
        valid_at[k] = valid_of(rows_at[k])
    own = rows_at[0]

    early = {}
    late = {}

    def add(sums_by_target, target, source, sums):
        sums_by_target.setdefault(target, []).append((source, sums))

    e = pair_products(own, own)
    add(early, 0, 0, jnp.sum(e * valid_at[0][None, :], axis=1))
    plan = [(0, 1), (0, 2), (0, 3), (-2, 2), (-2, 3), (-3, 3), (-4, 3)]
    for p, q in plan:
        e = pair_products(rows_at[p], rows_at[q])
        to_p = jnp.sum(e * valid_at[q][None, :], axis=1)
        to_q = jnp.sum(e * valid_at[p][:, None], axis=0)
        group = late if max(-p, q) == reach else early
        add(group, p, q, to_p)
        add(group, q, p, to_q)
    e = pair_products(rows_at[-reach], rows_at[reach])
    add(late, -reach, reach, jnp.sum(e * valid_at[reach][None, :], axis=1))

    def weighted(stacked, items, target):
        sources = (me + jnp.array([s - target for s, _ in items], jnp.int32)) % grp_count
        return jnp.sum(stacked * member[sources][:, None], axis=0)

    slot_sums = weighted(jnp.stack([s for _, s in early[0]]), early[0], 0)

    depth = max(len(items) for t, items in early.items() if t != 0)
    zero = jnp.zeros((BLK,), jnp.float32)
    table = [[zero] * depth for _ in range(grp_count)]
    source_table = [[0] * depth for _ in range(grp_count)]
    present_table = [[0.0] * depth for _ in range(grp_count)]
    for target, items in early.items():
        if target == 0:
            continue
        for k, (source, sums) in enumerate(items):
            table[target % grp_count][k] = sums
            source_table[target % grp_count][k] = source - target
            present_table[target % grp_count][k] = 1.0
    by_offset = jnp.stack([jnp.stack(row) for row in table])
    by_device = by_offset[(blocks_iota - me) % grp_count]
    arrived_sums = lax.all_to_all(by_device, "grp", split_axis=0, concat_axis=0, tiled=True)
    offset_of_sender = (me - blocks_iota) % grp_count
    sources = (me + jnp.array(source_table, jnp.int32)[offset_of_sender]) % grp_count
    weights = member[sources] * jnp.array(present_table, jnp.float32)[offset_of_sender]
    slot_sums = slot_sums + jnp.sum(arrived_sums * weights[:, :, None], axis=(0, 1))

    for target, items in sorted(late.items()):
        stacked = shift(jnp.stack([s for _, s in items]), target)
        slot_sums = slot_sums + weighted(stacked, items, target)

    own_valid = valid_at[0].reshape(2, wide_count, split).transpose(1, 0, 2).reshape(wide_count, capacity)
    arrived = jnp.sum(own_valid, axis=1).astype(jnp.int32)
    offsets = jnp.cumsum(arrived) - arrived
    within = jnp.arange(capacity, dtype=jnp.int32)
    places = jnp.where(own_valid > 0, offsets[:, None] + within[None, :], BLK)
    places = places.reshape(wide_count, 2, split).transpose(1, 0, 2).reshape(-1)
    rows_iota = jnp.arange(BLK, dtype=jnp.int32)
    density = jnp.sum(jnp.where(places[:, None] == rows_iota[None, :], slot_sums[:, None], 0.0), axis=0)
    return density.reshape(1, BLK)


def solution(mesh):
    placed = (P(("wide", "grp"), None), P(("wide", "grp")), P(("wide", "grp")))
    return jax.shard_map(
        per_device, mesh=mesh, in_specs=placed, out_specs=P(("wide", "grp"), None), check_vma=False
    )
```

```python
import jax
import jax.numpy as jnp
from jax import lax
from jax.sharding import PartitionSpec as P


BLK = 384


SHARPNESS = 10.0
EPSILON = 1e-06
SENTINEL = 2.0


def pair_products(left_rows, right_rows):
    cosines = lax.dot_general(
        left_rows, right_rows, (((1,), (1,)), ((), ())), preferred_element_type=jnp.float32
    )
    return jnp.exp(SHARPNESS * (cosines - 1.0))


def per_device(embeds, bucket, pairs):
    wide_count = lax.axis_size("wide")
    grp_count = lax.axis_size("grp")
    feature_width = embeds.shape[1]
    capacity = BLK // wide_count
    me = lax.axis_index("grp")

    blocks_iota = jnp.arange(grp_count, dtype=jnp.int32)
    member = jnp.any(pairs[:, None] == blocks_iota[None, :], axis=0).astype(jnp.float32)

    floats = embeds.astype(jnp.float32)
    unit_rows = (
        floats * lax.rsqrt(jnp.sum(floats * floats, axis=1, keepdims=True) + EPSILON)
    ).astype(jnp.bfloat16)
    onehot = (bucket[:, None] == jnp.arange(wide_count, dtype=jnp.int32)[None, :]).astype(jnp.int32)
    row_ranks = jnp.sum(jnp.cumsum(onehot, axis=0) * onehot, axis=1) - 1
    send_slots = bucket * capacity + row_ranks
    empty = jnp.zeros((wide_count * capacity, feature_width), jnp.bfloat16).at[:, 0].set(SENTINEL)
    outgoing = empty.at[send_slots].set(unit_rows).reshape(wide_count, capacity, feature_width)
    parts = 1
    split = capacity // parts
    halves = [outgoing[:, k * split:(k + 1) * split] for k in range(parts)]
    own_halves = [
        lax.all_to_all(h, "wide", split_axis=0, concat_axis=0, tiled=True).reshape(-1, feature_width)
        for h in halves
    ]

    def valid_of(rows):
        return (rows[:, 0].astype(jnp.float32) < 1.5).astype(jnp.float32)

    def shift(value, offset):
        return lax.ppermute(
            value, "grp", [(i, (i + offset) % grp_count) for i in range(grp_count)]
        )

    reach = 4
    rows_at = {}
    for part in own_halves:
        left = part
        right = part
        rows_at.setdefault(0, []).append(part)
        for step in range(1, reach + 1):
            left = shift(left, 1)
            right = shift(right, -1)
            rows_at.setdefault(-step, []).append(left)
            rows_at.setdefault(step, []).append(right)
    halves_at = rows_at
    rows_at = {}
    valid_at = {}
    for k, v in halves_at.items():
        rows_at[k] = jnp.concatenate(v, axis=0)
        valid_at[k] = valid_of(rows_at[k])
    own = rows_at[0]

    early = {}
    late = {}

    def add(sums_by_target, target, source, sums):
        sums_by_target.setdefault(target, []).append((source, sums))

    e = pair_products(own, own)
    add(early, 0, 0, jnp.sum(e * valid_at[0][None, :], axis=1))
    plan = [(0, 1), (0, 2), (0, 3), (-2, 2), (-2, 3), (-3, 3), (-4, 3)]
    for p, q in plan:
        e = pair_products(rows_at[p], rows_at[q])
        to_p = jnp.sum(e * valid_at[q][None, :], axis=1)
        to_q = jnp.sum(e * valid_at[p][:, None], axis=0)
        group = late if max(-p, q) == reach else early
        add(group, p, q, to_p)
        add(group, q, p, to_q)
    e = pair_products(rows_at[-reach], rows_at[reach])
    add(late, -reach, reach, jnp.sum(e * valid_at[reach][None, :], axis=1))

    def weighted(stacked, items, target):
        sources = (me + jnp.array([s - target for s, _ in items], jnp.int32)) % grp_count
        return jnp.sum(stacked * member[sources][:, None], axis=0)

    slot_sums = weighted(jnp.stack([s for _, s in early[0]]), early[0], 0)

    depth = max(len(items) for t, items in early.items() if t != 0)
    zero = jnp.zeros((BLK,), jnp.float32)
    table = [[zero] * depth for _ in range(grp_count)]
    source_table = [[0] * depth for _ in range(grp_count)]
    present_table = [[0.0] * depth for _ in range(grp_count)]
    for target, items in early.items():
        if target == 0:
            continue
        for k, (source, sums) in enumerate(items):
            table[target % grp_count][k] = sums
            source_table[target % grp_count][k] = source - target
            present_table[target % grp_count][k] = 1.0
    by_offset = jnp.stack([jnp.stack(row) for row in table])
    by_device = by_offset[(blocks_iota - me) % grp_count]
    arrived_sums = lax.all_to_all(by_device, "grp", split_axis=0, concat_axis=0, tiled=True)
    offset_of_sender = (me - blocks_iota) % grp_count
    sources = (me + jnp.array(source_table, jnp.int32)[offset_of_sender]) % grp_count
    weights = member[sources] * jnp.array(present_table, jnp.float32)[offset_of_sender]
    slot_sums = slot_sums + jnp.sum(arrived_sums * weights[:, :, None], axis=(0, 1))

    for target, items in sorted(late.items()):
        stacked = shift(jnp.stack([s for _, s in items]), target)
        slot_sums = slot_sums + weighted(stacked, items, target)

    own_valid = valid_at[0].reshape(parts, wide_count, split).transpose(1, 0, 2).reshape(wide_count, capacity)
    arrived = jnp.sum(own_valid, axis=1).astype(jnp.int32)
    offsets = jnp.cumsum(arrived) - arrived
    within = jnp.arange(capacity, dtype=jnp.int32)
    places = jnp.where(own_valid > 0, offsets[:, None] + within[None, :], BLK)
    places = places.reshape(wide_count, parts, split).transpose(1, 0, 2).reshape(-1)
    rows_iota = jnp.arange(BLK, dtype=jnp.int32)
    density = jnp.sum(jnp.where(places[:, None] == rows_iota[None, :], slot_sums[:, None], 0.0), axis=0)
    return density.reshape(1, BLK)


def solution(mesh):
    placed = (P(("wide", "grp"), None), P(("wide", "grp")), P(("wide", "grp")))
    return jax.shard_map(per_device, mesh=mesh, in_specs=placed, out_specs=P(("wide", "grp"), None), check_vma=False)
```

```python
import jax
import jax.numpy as jnp
import numpy as np
from jax import lax
from jax.sharding import PartitionSpec as P


BLK = 384


SHARPNESS = 10.0
EPSILON = 1e-06
SENTINEL = 2.0


def pair_products(left_rows, right_rows):
    cosines = lax.dot_general(
        left_rows, right_rows, (((1,), (1,)), ((), ())), preferred_element_type=jnp.float32
    )
    return jnp.exp(SHARPNESS * (cosines - 1.0))


def per_device(embeds, bucket, pairs):
    wide_count = lax.axis_size("wide")
    grp_count = lax.axis_size("grp")
    feature_width = embeds.shape[1]
    capacity = BLK // wide_count
    me = lax.axis_index("grp")

    blocks_iota = jnp.arange(grp_count, dtype=jnp.int32)
    relative = (pairs - me) % grp_count
    near = jnp.any(
        (relative[:, None] == blocks_iota[None, :]) & (pairs >= 0)[:, None], axis=0
    ).astype(jnp.float32)

    floats = embeds.astype(jnp.float32)
    unit_rows = (
        floats * lax.rsqrt(jnp.sum(floats * floats, axis=1, keepdims=True) + EPSILON)
    ).astype(jnp.bfloat16)
    onehot = (bucket[:, None] == jnp.arange(wide_count, dtype=jnp.int32)[None, :]).astype(jnp.int32)
    row_ranks = jnp.sum(jnp.cumsum(onehot, axis=0) * onehot, axis=1) - 1
    send_slots = bucket * capacity + row_ranks
    sentinel_row = jnp.where(jnp.arange(feature_width) == 0, SENTINEL, 0.0).astype(jnp.float32)
    parts = 3
    split = capacity // parts
    halves = []
    for h in range(parts):
        slot_ids = (
            jnp.arange(wide_count, dtype=jnp.int32)[:, None] * capacity
            + h * split
            + jnp.arange(split, dtype=jnp.int32)[None, :]
        ).reshape(-1)
        hits = slot_ids[:, None] == send_slots[None, :]
        placed_rows = lax.dot_general(
            hits.astype(jnp.bfloat16), unit_rows, (((1,), (0,)), ((), ())),
            preferred_element_type=jnp.float32,
        )
        filled = jnp.any(hits, axis=1)
        part = jnp.where(filled[:, None], placed_rows, sentinel_row[None, :]).astype(jnp.bfloat16)
        halves.append(part.reshape(wide_count, split, feature_width))
    own_halves = [
        lax.all_to_all(h, "wide", split_axis=0, concat_axis=0, tiled=True).reshape(-1, feature_width)
        for h in halves
    ]

    def valid_of(rows):
        return (rows[:, 0].astype(jnp.float32) < 1.5).astype(jnp.float32)

    def shift(value, offset):
        return lax.ppermute(
            value, "grp", [(i, (i + offset) % grp_count) for i in range(grp_count)]
        )

    reach = 4
    rows_at = {}
    for part in own_halves:
        left = part
        right = part
        rows_at.setdefault(0, []).append(part)
        for step in range(1, reach + 1):
            left = shift(left, 1)
            right = shift(right, -1)
            rows_at.setdefault(-step, []).append(left)
            rows_at.setdefault(step, []).append(right)
    halves_at = rows_at
    rows_at = {}
    valid_at = {}
    for k, v in halves_at.items():
        rows_at[k] = jnp.concatenate(v, axis=0)
        valid_at[k] = valid_of(rows_at[k])
    own = rows_at[0]

    early = {}
    late = {}

    def add(sums_by_target, target, source, sums):
        sums_by_target.setdefault(target, []).append((source, sums))

    e = pair_products(own, own)
    add(early, 0, 0, jnp.sum(e * valid_at[0][None, :], axis=1))
    plan = [(0, 1), (0, 2), (0, 3), (-2, 2), (-2, 3), (-3, 3), (-4, 3)]
    for p, q in plan:
        e = pair_products(rows_at[p], rows_at[q])
        to_p = jnp.sum(e * valid_at[q][None, :], axis=1)
        to_q = jnp.sum(e * valid_at[p][:, None], axis=0)
        group = late if max(-p, q) == reach else early
        add(group, p, q, to_p)
        add(group, q, p, to_q)
    e = pair_products(rows_at[-reach], rows_at[reach])
    add(late, -reach, reach, jnp.sum(e * valid_at[reach][None, :], axis=1))

    def near_at(offsets):
        hits = (np.asarray(offsets)[..., None] % grp_count) == np.arange(grp_count)
        return jnp.sum(jnp.asarray(hits, jnp.float32) * near, axis=-1)

    def weighted(stacked, items, target):
        weights = near_at([s - target for s, _ in items])
        return jnp.sum(stacked * weights[:, None], axis=0)

    slot_sums = weighted(jnp.stack([s for _, s in early[0]]), early[0], 0)

    depth = max(len(items) for t, items in early.items() if t != 0)
    zero = jnp.zeros((BLK,), jnp.float32)
    table = [[zero] * depth for _ in range(grp_count)]
    source_table = [[0] * depth for _ in range(grp_count)]
    present_table = [[0.0] * depth for _ in range(grp_count)]
    for target, items in early.items():
        if target == 0:
            continue
        for k, (source, sums) in enumerate(items):
            table[target % grp_count][k] = sums
            source_table[target % grp_count][k] = source - target
            present_table[target % grp_count][k] = 1.0
    by_offset = jnp.stack([jnp.stack(row) for row in table])
    start = (grp_count - me) % grp_count
    by_device = lax.dynamic_slice_in_dim(
        jnp.concatenate([by_offset, by_offset], axis=0), start, grp_count, 0
    )
    arrived_sums = lax.all_to_all(by_device, "grp", split_axis=0, concat_axis=0, tiled=True)
    gap_order = [(-g) % grp_count for g in range(grp_count)]
    by_gap = near_at(np.asarray(source_table)[gap_order]) * jnp.asarray(
        np.asarray(present_table, np.float32)[gap_order]
    )
    weights = lax.dynamic_slice_in_dim(jnp.concatenate([by_gap, by_gap], axis=0), start, grp_count, 0)
    slot_sums = slot_sums + jnp.sum(arrived_sums * weights[:, :, None], axis=(0, 1))

    for target, items in sorted(late.items()):
        stacked = shift(jnp.stack([s for _, s in items]), target)
        slot_sums = slot_sums + weighted(stacked, items, target)

    own_valid = valid_at[0].reshape(parts, wide_count, split).transpose(1, 0, 2).reshape(wide_count, capacity)
    arrived = jnp.sum(own_valid, axis=1).astype(jnp.int32)
    offsets = jnp.cumsum(arrived) - arrived
    within = jnp.arange(capacity, dtype=jnp.int32)
    places = jnp.where(own_valid > 0, offsets[:, None] + within[None, :], BLK)
    places = places.reshape(wide_count, parts, split).transpose(1, 0, 2).reshape(-1)
    rows_iota = jnp.arange(BLK, dtype=jnp.int32)
    density = jnp.sum(jnp.where(places[:, None] == rows_iota[None, :], slot_sums[:, None], 0.0), axis=0)
    return density.reshape(1, BLK)


def solution(mesh):
    placed = (P(("wide", "grp"), None), P(("wide", "grp")), P(("wide", "grp")))
    return jax.shard_map(per_device, mesh=mesh, in_specs=placed, out_specs=P(("wide", "grp"), None), check_vma=False)
```

```python
import jax
import jax.numpy as jnp
import numpy as np
from jax import lax
from jax.sharding import PartitionSpec as P


BLK = 384


SHARPNESS = 10.0
EPSILON = 1e-06
SENTINEL = 2.0


def pair_products(left_rows, right_rows):
    cosines = lax.dot_general(
        left_rows, right_rows, (((1,), (1,)), ((), ())), preferred_element_type=jnp.float32
    )
    return jnp.exp(SHARPNESS * (cosines - 1.0))


def per_device(embeds, bucket, pairs):
    wide_count = lax.axis_size("wide")
    grp_count = lax.axis_size("grp")
    feature_width = embeds.shape[1]
    capacity = BLK // wide_count
    me = lax.axis_index("grp")

    blocks_iota = jnp.arange(grp_count, dtype=jnp.int32)
    relative = (pairs - me) % grp_count
    near = jnp.any(
        (relative[:, None] == blocks_iota[None, :]) & (pairs >= 0)[:, None], axis=0
    ).astype(jnp.float32)

    floats = embeds.astype(jnp.float32)
    unit_rows = (
        floats * lax.rsqrt(jnp.sum(floats * floats, axis=1, keepdims=True) + EPSILON)
    ).astype(jnp.bfloat16)
    onehot = (bucket[:, None] == jnp.arange(wide_count, dtype=jnp.int32)[None, :]).astype(jnp.int32)
    row_ranks = jnp.sum(jnp.cumsum(onehot, axis=0) * onehot, axis=1) - 1
    send_slots = bucket * capacity + row_ranks
    sentinel_row = jnp.where(jnp.arange(feature_width) == 0, SENTINEL, 0.0).astype(jnp.float32)
    split = capacity // 2
    halves = []
    for h in range(2):
        slot_ids = (
            jnp.arange(wide_count, dtype=jnp.int32)[:, None] * capacity
            + h * split
            + jnp.arange(split, dtype=jnp.int32)[None, :]
        ).reshape(-1)
        hits = slot_ids[:, None] == send_slots[None, :]
        placed_rows = lax.dot_general(
            hits.astype(jnp.bfloat16), unit_rows, (((1,), (0,)), ((), ())),
            preferred_element_type=jnp.float32,
        )
        filled = jnp.any(hits, axis=1)
        part = jnp.where(filled[:, None], placed_rows, sentinel_row[None, :]).astype(jnp.bfloat16)
        halves.append(part.reshape(wide_count, split, feature_width))
    own_halves = [
        lax.all_to_all(h, "wide", split_axis=0, concat_axis=0, tiled=True).reshape(-1, feature_width)
        for h in halves
    ]

    def valid_of(rows):
        return (rows[:, 0].astype(jnp.float32) < 1.5).astype(jnp.float32)

    def shift(value, offset):
        return lax.ppermute(
            value, "grp", [(i, (i + offset) % grp_count) for i in range(grp_count)]
        )

    reach = 4
    rows_at = {}
    for part in own_halves:
        left = part
        right = part
        rows_at.setdefault(0, []).append(part)
        for step in range(1, reach + 1):
            left = shift(left, 1)
            right = shift(right, -1)
            rows_at.setdefault(-step, []).append(left)
            rows_at.setdefault(step, []).append(right)
    halves_at = rows_at
    rows_at = {}
    valid_at = {}
    for k, v in halves_at.items():
        rows_at[k] = jnp.concatenate(v, axis=0)
        valid_at[k] = valid_of(rows_at[k])
    own = rows_at[0]

    early = {}
    late = {}

    def add(sums_by_target, target, source, sums):
        sums_by_target.setdefault(target, []).append((source, sums))

    e = pair_products(own, own)
    add(early, 0, 0, jnp.sum(e * valid_at[0][None, :], axis=1))
    plan = [(0, 1), (0, 2), (0, 3), (-2, 2), (-2, 3), (-3, 3), (-4, 3)]
    for p, q in plan:
        e = pair_products(rows_at[p], rows_at[q])
        to_p = jnp.sum(e * valid_at[q][None, :], axis=1)
        to_q = jnp.sum(e * valid_at[p][:, None], axis=0)
        group = late if max(-p, q) == reach else early
        add(group, p, q, to_p)
        add(group, q, p, to_q)
    e = pair_products(rows_at[-reach], rows_at[reach])
    add(late, -reach, reach, jnp.sum(e * valid_at[reach][None, :], axis=1))

    def near_at(offsets):
        hits = (np.asarray(offsets)[..., None] % grp_count) == np.arange(grp_count)
        return jnp.sum(jnp.asarray(hits, jnp.float32) * near, axis=-1)

    def weighted(stacked, items, target):
        weights = near_at([s - target for s, _ in items])
        return jnp.sum(stacked * weights[:, None], axis=0)

    slot_sums = weighted(jnp.stack([s for _, s in early[0]]), early[0], 0)

    depth = max(len(items) for t, items in early.items() if t != 0)
    zero = jnp.zeros((BLK,), jnp.float32)
    table = [[zero] * depth for _ in range(grp_count)]
    source_table = [[0] * depth for _ in range(grp_count)]
    present_table = [[0.0] * depth for _ in range(grp_count)]
    for target, items in early.items():
        if target == 0:
            continue
        for k, (source, sums) in enumerate(items):
            table[target % grp_count][k] = sums
            source_table[target % grp_count][k] = source - target
            present_table[target % grp_count][k] = 1.0
    by_offset = jnp.stack([jnp.stack(row) for row in table])
    start = (grp_count - me) % grp_count
    by_device = lax.dynamic_slice_in_dim(
        jnp.concatenate([by_offset, by_offset], axis=0), start, grp_count, 0
    )
    arrived_sums = lax.all_to_all(by_device, "grp", split_axis=0, concat_axis=0, tiled=True)
    gap_order = [(-g) % grp_count for g in range(grp_count)]
    by_gap = near_at(np.asarray(source_table)[gap_order]) * jnp.asarray(
        np.asarray(present_table, np.float32)[gap_order]
    )
    weights = lax.dynamic_slice_in_dim(jnp.concatenate([by_gap, by_gap], axis=0), start, grp_count, 0)
    slot_sums = slot_sums + jnp.sum(arrived_sums * weights[:, :, None], axis=(0, 1))

    for target, items in sorted(late.items()):
        stacked = shift(jnp.stack([s for _, s in items]), target)
        slot_sums = slot_sums + weighted(stacked, items, target)

    own_valid = valid_at[0].reshape(2, wide_count, split).transpose(1, 0, 2).reshape(wide_count, capacity)
    arrived = jnp.sum(own_valid, axis=1).astype(jnp.int32)
    offsets = jnp.cumsum(arrived) - arrived
    within = jnp.arange(capacity, dtype=jnp.int32)
    places = jnp.where(own_valid > 0, offsets[:, None] + within[None, :], BLK)
    places = places.reshape(wide_count, 2, split).transpose(1, 0, 2).reshape(-1)
    rows_iota = jnp.arange(BLK, dtype=jnp.int32)
    density = jnp.sum(jnp.where(places[:, None] == rows_iota[None, :], slot_sums[:, None], 0.0), axis=0)
    return density.reshape(1, BLK)


def solution(mesh):
    placed = (P(("wide", "grp"), None), P(("wide", "grp")), P(("wide", "grp")))
    return jax.shard_map(per_device, mesh=mesh, in_specs=placed, out_specs=P(("wide", "grp"), None), check_vma=False)
```

```python
import jax
import jax.numpy as jnp
import numpy as np
from jax import lax
from jax.sharding import PartitionSpec as P


BLK = 384


SHARPNESS = 10.0
EPSILON = 1e-06
SENTINEL = 2.0


def pair_products(left_rows, right_rows):
    cosines = lax.dot_general(
        left_rows, right_rows, (((1,), (1,)), ((), ())), preferred_element_type=jnp.float32
    )
    return jnp.exp(SHARPNESS * (cosines - 1.0))


def per_device(embeds, bucket, pairs):
    wide_count = lax.axis_size("wide")
    grp_count = lax.axis_size("grp")
    feature_width = embeds.shape[1]
    capacity = BLK // wide_count
    me = lax.axis_index("grp")

    blocks_iota = jnp.arange(grp_count, dtype=jnp.int32)
    relative = (pairs - me) % grp_count
    near = jnp.any(
        (relative[:, None] == blocks_iota[None, :]) & (pairs >= 0)[:, None], axis=0
    ).astype(jnp.float32)

    floats = embeds.astype(jnp.float32)
    unit_rows = (
        floats * lax.rsqrt(jnp.sum(floats * floats, axis=1, keepdims=True) + EPSILON)
    ).astype(jnp.bfloat16)
    onehot = (bucket[:, None] == jnp.arange(wide_count, dtype=jnp.int32)[None, :]).astype(jnp.int32)
    row_ranks = jnp.sum(jnp.cumsum(onehot, axis=0) * onehot, axis=1) - 1
    send_slots = bucket * capacity + row_ranks
    sentinel_row = jnp.where(jnp.arange(feature_width) == 0, SENTINEL, 0.0).astype(jnp.float32)
    split = capacity // 2
    halves = []
    for h in range(2):
        slot_ids = (
            jnp.arange(wide_count, dtype=jnp.int32)[:, None] * capacity
            + h * split
            + jnp.arange(split, dtype=jnp.int32)[None, :]
        ).reshape(-1)
        hits = slot_ids[:, None] == send_slots[None, :]
        placed_rows = lax.dot_general(
            hits.astype(jnp.bfloat16), unit_rows, (((1,), (0,)), ((), ())),
            preferred_element_type=jnp.float32,
        )
        filled = jnp.any(hits, axis=1)
        part = jnp.where(filled[:, None], placed_rows, sentinel_row[None, :]).astype(jnp.bfloat16)
        halves.append(part.reshape(wide_count, split, feature_width))
    own_halves = [
        lax.all_to_all(h, "wide", split_axis=0, concat_axis=0, tiled=True).reshape(-1, feature_width)
        for h in halves
    ]

    def valid_of(rows):
        return (rows[:, 0].astype(jnp.float32) < 1.5).astype(jnp.float32)

    def shift(value, offset):
        return lax.ppermute(
            value, "grp", [(i, (i + offset) % grp_count) for i in range(grp_count)]
        )

    reach = 5
    reach_right = 3
    rows_at = {}
    for part in own_halves:
        left = part
        right = part
        rows_at.setdefault(0, []).append(part)
        for step in range(1, reach + 1):
            left = shift(left, 1)
            rows_at.setdefault(-step, []).append(left)
            if step <= reach_right:
                right = shift(right, -1)
                rows_at.setdefault(step, []).append(right)
    halves_at = rows_at
    rows_at = {}
    valid_at = {}
    for k, v in halves_at.items():
        rows_at[k] = jnp.concatenate(v, axis=0)
        valid_at[k] = valid_of(rows_at[k])
    own = rows_at[0]

    early = {}
    late = {}

    def add(sums_by_target, target, source, sums):
        sums_by_target.setdefault(target, []).append((source, sums))

    e = pair_products(own, own)
    add(early, 0, 0, jnp.sum(e * valid_at[0][None, :], axis=1))
    plan = [(0, 1), (0, 2), (0, 3), (-2, 2), (-2, 3), (-3, 3), (-4, 3)]
    for p, q in plan:
        e = pair_products(rows_at[p], rows_at[q])
        to_p = jnp.sum(e * valid_at[q][None, :], axis=1)
        to_q = jnp.sum(e * valid_at[p][:, None], axis=0)
        add(early, p, q, to_p)
        add(early, q, p, to_q)
    e = pair_products(rows_at[-reach], rows_at[reach_right])
    add(late, -reach, reach_right, jnp.sum(e * valid_at[reach_right][None, :], axis=1))

    def near_at(offsets):
        hits = (np.asarray(offsets)[..., None] % grp_count) == np.arange(grp_count)
        return jnp.sum(jnp.asarray(hits, jnp.float32) * near, axis=-1)

    def weighted(stacked, items, target):
        weights = near_at([s - target for s, _ in items])
        return jnp.sum(stacked * weights[:, None], axis=0)

    slot_sums = weighted(jnp.stack([s for _, s in early[0]]), early[0], 0)

    depth = max(len(items) for t, items in early.items() if t != 0)
    zero = jnp.zeros((BLK,), jnp.float32)
    table = [[zero] * depth for _ in range(grp_count)]
    source_table = [[0] * depth for _ in range(grp_count)]
    present_table = [[0.0] * depth for _ in range(grp_count)]
    for target, items in early.items():
        if target == 0:
            continue
        for k, (source, sums) in enumerate(items):
            table[target % grp_count][k] = sums
            source_table[target % grp_count][k] = source - target
            present_table[target % grp_count][k] = 1.0
    by_offset = jnp.stack([jnp.stack(row) for row in table])
    start = (grp_count - me) % grp_count
    by_device = lax.dynamic_slice_in_dim(
        jnp.concatenate([by_offset, by_offset], axis=0), start, grp_count, 0
    )
    arrived_sums = lax.all_to_all(by_device, "grp", split_axis=0, concat_axis=0, tiled=True)
    gap_order = [(-g) % grp_count for g in range(grp_count)]
    by_gap = near_at(np.asarray(source_table)[gap_order]) * jnp.asarray(
        np.asarray(present_table, np.float32)[gap_order]
    )
    weights = lax.dynamic_slice_in_dim(jnp.concatenate([by_gap, by_gap], axis=0), start, grp_count, 0)
    slot_sums = slot_sums + jnp.sum(arrived_sums * weights[:, :, None], axis=(0, 1))

    for target, items in sorted(late.items()):
        stacked = shift(jnp.stack([s for _, s in items]), target)
        slot_sums = slot_sums + weighted(stacked, items, target)

    own_valid = valid_at[0].reshape(2, wide_count, split).transpose(1, 0, 2).reshape(wide_count, capacity)
    arrived = jnp.sum(own_valid, axis=1).astype(jnp.int32)
    offsets = jnp.cumsum(arrived) - arrived
    within = jnp.arange(capacity, dtype=jnp.int32)
    places = jnp.where(own_valid > 0, offsets[:, None] + within[None, :], BLK)
    places = places.reshape(wide_count, 2, split).transpose(1, 0, 2).reshape(-1)
    rows_iota = jnp.arange(BLK, dtype=jnp.int32)
    density = jnp.sum(jnp.where(places[:, None] == rows_iota[None, :], slot_sums[:, None], 0.0), axis=0)
    return density.reshape(1, BLK)


def solution(mesh):
    placed = (P(("wide", "grp"), None), P(("wide", "grp")), P(("wide", "grp")))
    return jax.shard_map(per_device, mesh=mesh, in_specs=placed, out_specs=P(("wide", "grp"), None), check_vma=False)
```

```python
import jax
import jax.numpy as jnp
from jax import lax
from jax.sharding import PartitionSpec as P


BLK = 384


SHARPNESS = 10.0
EPSILON = 1e-06
SENTINEL = 2.0


def pair_products(left_rows, right_rows):
    cosines = lax.dot_general(
        left_rows, right_rows, (((1,), (1,)), ((), ())), preferred_element_type=jnp.float32
    )
    return jnp.exp(SHARPNESS * (cosines - 1.0))


def per_device(embeds, bucket, pairs):
    wide_count = lax.axis_size("wide")
    grp_count = lax.axis_size("grp")
    feature_width = embeds.shape[1]
    capacity = BLK // wide_count
    me = lax.axis_index("grp")

    blocks_iota = jnp.arange(grp_count, dtype=jnp.int32)
    relative = (pairs - me) % grp_count
    near = jnp.any(
        (relative[:, None] == blocks_iota[None, :]) & (pairs >= 0)[:, None], axis=0
    ).astype(jnp.float32)

    floats = embeds.astype(jnp.float32)
    unit_rows = (
        floats * lax.rsqrt(jnp.sum(floats * floats, axis=1, keepdims=True) + EPSILON)
    ).astype(jnp.bfloat16)
    onehot = (bucket[:, None] == jnp.arange(wide_count, dtype=jnp.int32)[None, :]).astype(jnp.int32)
    row_ranks = jnp.sum(jnp.cumsum(onehot, axis=0) * onehot, axis=1) - 1
    send_slots = bucket * capacity + row_ranks
    sentinel_row = jnp.where(jnp.arange(feature_width) == 0, SENTINEL, 0.0).astype(jnp.float32)
    split = capacity // 2
    halves = []
    for h in range(2):
        slot_ids = (
            jnp.arange(wide_count, dtype=jnp.int32)[:, None] * capacity
            + h * split
            + jnp.arange(split, dtype=jnp.int32)[None, :]
        ).reshape(-1)
        hits = slot_ids[:, None] == send_slots[None, :]
        placed_rows = lax.dot_general(
            hits.astype(jnp.bfloat16), unit_rows, (((1,), (0,)), ((), ())),
            preferred_element_type=jnp.float32,
        )
        filled = jnp.any(hits, axis=1)
        part = jnp.where(filled[:, None], placed_rows, sentinel_row[None, :]).astype(jnp.bfloat16)
        halves.append(part.reshape(wide_count, split, feature_width))
    own_halves = [
        lax.all_to_all(h, "wide", split_axis=0, concat_axis=0, tiled=True).reshape(-1, feature_width)
        for h in halves
    ]

    def valid_of(rows):
        return (rows[:, 0].astype(jnp.float32) < 1.5).astype(jnp.float32)

    def shift(value, offset):
        return lax.ppermute(
            value, "grp", [(i, (i + offset) % grp_count) for i in range(grp_count)]
        )

    reach = 4
    rows_at = {}
    for part in own_halves:
        left = part
        right = part
        rows_at.setdefault(0, []).append(part)
        for step in range(1, reach + 1):
            left = shift(left, 1)
            right = shift(right, -1)
            rows_at.setdefault(-step, []).append(left)
            rows_at.setdefault(step, []).append(right)
    halves_at = rows_at
    rows_at = {}
    valid_at = {}
    for k, v in halves_at.items():
        rows_at[k] = jnp.concatenate(v, axis=0)
        valid_at[k] = valid_of(rows_at[k])
    own = rows_at[0]

    early = {}
    late = {}

    def add(sums_by_target, target, source, sums):
        sums_by_target.setdefault(target, []).append((source, sums))

    e = pair_products(own, own)
    add(early, 0, 0, jnp.sum(e * valid_at[0][None, :], axis=1))
    plan = [(0, 1), (0, 2), (0, 3), (-2, 2), (-2, 3), (-3, 3), (-4, 3)]
    for p, q in plan:
        e = pair_products(rows_at[p], rows_at[q])
        to_p = jnp.sum(e * valid_at[q][None, :], axis=1)
        to_q = jnp.sum(e * valid_at[p][:, None], axis=0)
        group = late if max(-p, q) == reach else early
        add(group, p, q, to_p)
        add(group, q, p, to_q)
    e = pair_products(rows_at[-reach], rows_at[reach])
    add(late, -reach, reach, jnp.sum(e * valid_at[reach][None, :], axis=1))

    def weighted(stacked, items, target):
        weights = jnp.stack([near[(s - target) % grp_count] for s, _ in items])
        return jnp.sum(stacked * weights[:, None], axis=0)

    slot_sums = weighted(jnp.stack([s for _, s in early[0]]), early[0], 0)

    depth = max(len(items) for t, items in early.items() if t != 0)
    zero = jnp.zeros((BLK,), jnp.float32)
    table = [[zero] * depth for _ in range(grp_count)]
    source_table = [[0] * depth for _ in range(grp_count)]
    present_table = [[0.0] * depth for _ in range(grp_count)]
    for target, items in early.items():
        if target == 0:
            continue
        for k, (source, sums) in enumerate(items):
            table[target % grp_count][k] = sums
            source_table[target % grp_count][k] = source - target
            present_table[target % grp_count][k] = 1.0
    by_offset = jnp.stack([jnp.stack(row) for row in table])
    start = (grp_count - me) % grp_count
    by_device = lax.dynamic_slice_in_dim(
        jnp.concatenate([by_offset, by_offset], axis=0), start, grp_count, 0
    )
    arrived_sums = lax.all_to_all(by_device, "grp", split_axis=0, concat_axis=0, tiled=True)
    by_gap = jnp.stack([
        jnp.stack([
            near[source_table[(-g) % grp_count][k] % grp_count] * present_table[(-g) % grp_count][k]
            for k in range(depth)
        ])
        for g in range(grp_count)
    ])
    weights = lax.dynamic_slice_in_dim(jnp.concatenate([by_gap, by_gap], axis=0), start, grp_count, 0)
    slot_sums = slot_sums + jnp.sum(arrived_sums * weights[:, :, None], axis=(0, 1))

    for target, items in sorted(late.items()):
        stacked = shift(jnp.stack([s for _, s in items]), target)
        slot_sums = slot_sums + weighted(stacked, items, target)

    own_valid = valid_at[0].reshape(2, wide_count, split).transpose(1, 0, 2).reshape(wide_count, capacity)
    arrived = jnp.sum(own_valid, axis=1).astype(jnp.int32)
    offsets = jnp.cumsum(arrived) - arrived
    within = jnp.arange(capacity, dtype=jnp.int32)
    places = jnp.where(own_valid > 0, offsets[:, None] + within[None, :], BLK)
    places = places.reshape(wide_count, 2, split).transpose(1, 0, 2).reshape(-1)
    rows_iota = jnp.arange(BLK, dtype=jnp.int32)
    density = jnp.sum(jnp.where(places[:, None] == rows_iota[None, :], slot_sums[:, None], 0.0), axis=0)
    return density.reshape(1, BLK)


def solution(mesh):
    placed = (P(("wide", "grp"), None), P(("wide", "grp")), P(("wide", "grp")))
    return jax.shard_map(per_device, mesh=mesh, in_specs=placed, out_specs=P(("wide", "grp"), None), check_vma=False)
```
